32 devices in a mesh: grp: 4 (over z), band: 8 (over y, x, core).
Axes of the slice: x: 2, y: 2, z: 4, core: 2. Of those that a mesh axis runs over, the one named last changes fastest.
Arguments:
- orbitals: float32 [18432, 512], P('grp', 'band'), may hold values from -6 to 6
- requests: int32 [32, 6], replicated, may hold values from -1 to 11, as said below
- coulomb: float32 [96, 1536, 1536], P(('grp', 'band')), may hold values from -0.001953125 to 0.001953125
Outputs:
- exchange_rows: float32 [18432, 512], P('grp', 'band')
The draws below stay inside these ranges and needn't reach their ends.
Inputs may be any that keep to these rules, and one draw needn't show every extreme that they name: `requests`: entries 2q and 2q + 1 of row d are the two blocks of slot q of device d, the first not above the second, or both -1 for an empty slot; every pair of the 12 blocks, a block with itself included, stands in exactly one slot.
All inputs are finite; a program needn't handle non-finite values.
Results may differ from the reference program's by a relative error of at most 0.0003.
Values sent between devices are 32-bit elements; how exact they have to be, the bound alone decides.
No kernel may reach another device: no remote copies, remote signals or barrier semaphores. Data moves between devices by JAX's collectives and lax.ppermute only.
A program may use at most 256 MiB of HBM per device.

```python
import jax
import jax.numpy as jnp
import numpy as np
from jax import lax

N = 512
BLK = 1536
NB = 12
OWNERS = 32
Q = 3
POINTS = 18432
N_GRP = 4
N_BAND = 8


def draw_requests(key, part):
    upper_rows, upper_cols = np.triu_indices(NB)
    pair_table = jnp.stack([jnp.asarray(upper_rows, dtype=jnp.int32), jnp.asarray(upper_cols, dtype=jnp.int32)], 1)
    slot_total = OWNERS * Q
    empty_rows = jnp.full((slot_total - pair_table.shape[0], 2), -1, jnp.int32)
    padded = jnp.concatenate([pair_table, empty_rows], 0)
    order = jax.random.permutation(key, slot_total)
    return padded[order].reshape(OWNERS, 2 * Q)


def block_levels(key, shape, pieces, least, high):
    gain, own = 1.0, jax.random.fold_in(key, 6)
    for position, parts in pieces:
        draws = jnp.exp(jax.random.uniform(jax.random.fold_in(own, position), (parts,), jnp.float32, least / len(pieces), high / len(pieces)))
        gain = gain * jnp.repeat(draws, shape[position] // parts).reshape([-1 if axis == position else 1 for axis in range(len(shape))])
    return gain


def bell_draw(rng, shape, spread, reach, split=(), kind=jnp.bfloat16):
    drawn = jax.random.normal(rng, shape, jnp.float32) * spread
    if len(split) > 0:
        drawn = block_levels(rng, shape, split, -0.22, 0.18) * drawn
    return jnp.clip(drawn, min=-reach, max=reach).astype(kind)


def setup_inputs(seed: int = 0) -> dict:
    arg_keys = jax.random.split(jax.random.key(seed), 4)
    return {
        "orbitals": bell_draw(arg_keys[0], (POINTS, N), 1.0, 6.0, ((0, 4), (1, 8)), jnp.float32),
        "requests": draw_requests(jax.random.fold_in(arg_keys[3], 71), 0),
        "coulomb": bell_draw(arg_keys[2], (OWNERS * Q, BLK, BLK), (NB * BLK * N) ** -0.5, 0.001953125, ((0, 32),), jnp.float32),
    }


def slot_work(first_block, second_block, coulomb_tile, diagonal):
    density = jnp.dot(first_block, second_block.T, precision=lax.Precision.HIGHEST, preferred_element_type=jnp.float32)
    symmetric = jnp.where(diagonal, 0.5 * (coulomb_tile + coulomb_tile.T), coulomb_tile)
    kernel = density * symmetric
    onto_first = jnp.dot(kernel, second_block, precision=lax.Precision.HIGHEST, preferred_element_type=jnp.float32)
    onto_second = jnp.dot(kernel.T, first_block, precision=lax.Precision.HIGHEST, preferred_element_type=jnp.float32)
    onto_second = onto_second * jnp.where(diagonal, 0.0, 1.0)
    return jnp.stack([onto_first, onto_second], 0)


def reference(orbitals, requests, coulomb):
    devices = N_GRP * N_BAND
    piece_rows = BLK // devices
    blocks = orbitals.reshape(devices, NB, piece_rows, N).transpose(1, 0, 2, 3).reshape(NB, BLK, N)
    pair_ids = requests.reshape(devices * Q, 2)

    def slot_step(running, slot_item):
        pair_now, coulomb_tile = slot_item
        first_id = jnp.maximum(pair_now[0], 0).astype(jnp.int32)
        second_id = jnp.maximum(pair_now[1], 0).astype(jnp.int32)
        live_scale = jnp.where(pair_now[0] >= 0, 1.0, 0.0)
        first_block = blocks[first_id] * live_scale
        second_block = blocks[second_id] * live_scale
        both_terms = slot_work(first_block, second_block, coulomb_tile, pair_now[0] == pair_now[1])
        running = running.at[first_id].add(both_terms[0])
        running = running.at[second_id].add(both_terms[1])
        return running, None

    running = jnp.zeros((NB, BLK, N), jnp.float32)
    running = lax.scan(slot_step, running, (pair_ids, coulomb))[0]
    return running.reshape(NB, devices, piece_rows, N).transpose(1, 0, 2, 3).reshape(NB * BLK, N)
```

```python
import jax
import jax.numpy as jnp
from jax import lax
from jax.sharding import PartitionSpec as P


def slot_work(first_block, second_block, coulomb_tile, diagonal):
    density = jnp.dot(
        first_block,
        second_block.T,
        precision=lax.Precision.HIGHEST,
        preferred_element_type=jnp.float32,
    )
    symmetric = jnp.where(diagonal, 0.5 * (coulomb_tile + coulomb_tile.T), coulomb_tile)
    kernel = density * symmetric
    onto_first = jnp.dot(
        kernel, second_block, precision=lax.Precision.HIGHEST, preferred_element_type=jnp.float32
    )
    onto_second = jnp.dot(
        kernel.T, first_block, precision=lax.Precision.HIGHEST, preferred_element_type=jnp.float32
    )
    onto_second = onto_second * jnp.where(diagonal, 0.0, 1.0)
    return jnp.stack([onto_first, onto_second], 0)


def body(orbitals, requests, coulomb):
    group_count = lax.axis_size("grp")
    band_count = lax.axis_size("band")
    devices = group_count * band_count
    blk = coulomb.shape[1]
    col_width = orbitals.shape[1]
    orbital_width = col_width * band_count
    piece_rows = blk // devices
    all_points = lax.all_gather(orbitals, "grp", axis=0, tiled=True)
    block_count = all_points.shape[0] // (devices * piece_rows)
    blocks = (
        all_points.reshape(devices, block_count, piece_rows, col_width)
        .transpose(1, 0, 2, 3)
        .reshape(block_count, blk, col_width)
    )
    request_count = requests.shape[1]
    group_index = lax.axis_index("grp")
    band_index = lax.axis_index("band")
    group_requests = lax.dynamic_slice_in_dim(requests, group_index * band_count, band_count, 0)
    live = (group_requests >= 0).astype(jnp.float32)
    outgoing = jnp.take(blocks, jnp.maximum(group_requests, 0), axis=0) * live[:, :, None, None]
    arrived = lax.all_to_all(outgoing, "band", split_axis=0, concat_axis=0, tiled=True)
    fetched = arrived.transpose(1, 2, 0, 3).reshape(request_count // 2, 2, blk, orbital_width)
    own_pairs = lax.dynamic_index_in_dim(group_requests, band_index, 0, keepdims=False).reshape(
        request_count // 2, 2
    )
    diagonal = own_pairs[:, 0] == own_pairs[:, 1]

    def per_slot(slot_item):
        pair_rows, coulomb_tile, diag_flag = slot_item
        return slot_work(pair_rows[0], pair_rows[1], coulomb_tile, diag_flag)

    results = lax.map(per_slot, (fetched, coulomb, diagonal))
    outbound = results.reshape(request_count, blk, band_count, col_width).transpose(2, 0, 1, 3)
    returned = lax.all_to_all(outbound, "band", split_axis=0, concat_axis=0, tiled=True)
    one_hot = (
        group_requests[:, :, None] == jnp.arange(block_count, dtype=jnp.int32)[None, None, :]
    ).astype(jnp.float32)
    summed = jnp.einsum("srk,srpc->kpc", one_hot, returned, precision=lax.Precision.HIGHEST)
    summed = summed.reshape(block_count, group_count, band_count, piece_rows, col_width)
    mine = lax.psum_scatter(summed, "grp", scatter_dimension=1, tiled=True)
    mine = mine.reshape(block_count, band_count, piece_rows, col_width).transpose(1, 0, 2, 3)
    return mine.reshape(band_count * block_count * piece_rows, col_width)


def solution(mesh):
    placed = (P("grp", "band"), P(), P(("grp", "band"), None, None))
    return jax.shard_map(
        body, mesh=mesh, in_specs=placed, out_specs=P("grp", "band"), check_vma=False
    )
```

```python
import jax
import jax.numpy as jnp
from jax import lax
from jax.sharding import PartitionSpec as P

PRECISION = lax.Precision.HIGH


def slot_work(first_block, second_block, coulomb_tile, diagonal):
    density = jnp.dot(
        first_block, second_block.T, precision=PRECISION, preferred_element_type=jnp.float32
    )
    symmetric = jnp.where(diagonal, 0.5 * (coulomb_tile + coulomb_tile.T), coulomb_tile)
    kernel = density * symmetric
    onto_first = jnp.dot(kernel, second_block, precision=PRECISION, preferred_element_type=jnp.float32)
    onto_second = jnp.dot(kernel.T, first_block, precision=PRECISION, preferred_element_type=jnp.float32)
    onto_second = onto_second * jnp.where(diagonal, 0.0, 1.0)
    return jnp.stack([onto_first, onto_second], 0)


def body(orbitals, requests, coulomb):
    group_count = lax.axis_size("grp")
    band_count = lax.axis_size("band")
    devices = group_count * band_count
    blk = coulomb.shape[1]
    col_width = orbitals.shape[1]
    orbital_width = col_width * band_count
    piece_rows = blk // devices
    slot_count = coulomb.shape[0]
    copies = jnp.broadcast_to(orbitals[None], (group_count,) + orbitals.shape)
    all_points = lax.all_to_all(copies, "grp", split_axis=0, concat_axis=0, tiled=True)
    block_count = all_points.shape[0] * all_points.shape[1] // (devices * piece_rows)
    blocks = (
        all_points.reshape(devices, block_count, piece_rows, col_width)
        .transpose(1, 0, 2, 3)
        .reshape(block_count, blk, col_width)
    )
    group_index = lax.axis_index("grp")
    band_index = lax.axis_index("band")
    group_requests = lax.dynamic_slice_in_dim(requests, group_index * band_count, band_count, 0)
    live = (group_requests >= 0).astype(jnp.float32)
    own_pairs = lax.dynamic_index_in_dim(group_requests, band_index, 0, keepdims=False)
    returned = []
    for slot in range(slot_count):
        wanted = group_requests[:, 2 * slot : 2 * slot + 2]
        outgoing = jnp.take(blocks, jnp.maximum(wanted, 0), axis=0)
        outgoing = outgoing * live[:, 2 * slot : 2 * slot + 2, None, None]
        arrived = lax.all_to_all(outgoing, "band", split_axis=0, concat_axis=0, tiled=True)
        pair_rows = arrived.transpose(1, 2, 0, 3).reshape(2, blk, orbital_width)
        diagonal = own_pairs[2 * slot] == own_pairs[2 * slot + 1]
        result = slot_work(pair_rows[0], pair_rows[1], coulomb[slot], diagonal)
        outbound = result.reshape(2, blk, band_count, col_width).transpose(2, 0, 1, 3)
        returned.append(lax.all_to_all(outbound, "band", split_axis=0, concat_axis=0, tiled=True))
    returned = jnp.concatenate(returned, axis=1)
    one_hot = (
        group_requests[:, :, None] == jnp.arange(block_count, dtype=jnp.int32)[None, None, :]
    ).astype(jnp.float32)
    summed = jnp.einsum("srk,srpc->kpc", one_hot, returned, precision=lax.Precision.HIGHEST)
    summed = summed.reshape(block_count, group_count, band_count, piece_rows, col_width)
    summed = summed.transpose(1, 0, 2, 3, 4)
    parts = lax.all_to_all(summed, "grp", split_axis=0, concat_axis=0, tiled=True)
    mine = parts.sum(axis=0).transpose(1, 0, 2, 3)
    return mine.reshape(band_count * block_count * piece_rows, col_width)


def solution(mesh):
    placed = (P("grp", "band"), P(), P(("grp", "band"), None, None))
    return jax.shard_map(
        body, mesh=mesh, in_specs=placed, out_specs=P("grp", "band"), check_vma=False
    )
```

```python
import jax
import jax.numpy as jnp
from jax import lax
from jax.sharding import PartitionSpec as P

PRECISION = lax.Precision.HIGH
EXACT = lax.Precision.HIGHEST


def body(orbitals, requests, coulomb):
    group_count = lax.axis_size("grp")
    band_count = lax.axis_size("band")
    devices = group_count * band_count
    blk = coulomb.shape[1]
    col_width = orbitals.shape[1]
    piece_rows = blk // devices
    slot_count = coulomb.shape[0]
    block_count = orbitals.shape[0] // (band_count * piece_rows)
    copies = jnp.broadcast_to(orbitals[None], (group_count,) + orbitals.shape)
    all_points = lax.all_to_all(copies, "grp", split_axis=0, concat_axis=0, tiled=True)
    all_points = all_points.reshape(group_count, band_count, block_count, piece_rows, col_width)
    group_index = lax.axis_index("grp")
    band_index = lax.axis_index("band")
    group_requests = lax.dynamic_slice_in_dim(requests, group_index * band_count, band_count, 0)
    one_hot = (
        group_requests[:, :, None] == jnp.arange(block_count, dtype=jnp.int32)[None, None, :]
    ).astype(jnp.float32)
    own_pairs = lax.dynamic_index_in_dim(group_requests, band_index, 0, keepdims=False)
    summed = None
    for slot in range(slot_count):
        pick = one_hot[:, 2 * slot : 2 * slot + 2]
        outgoing = jnp.einsum("rqk,gjkpc->rqgjpc", pick, all_points, precision=EXACT)
        arrived = lax.all_to_all(outgoing, "band", split_axis=0, concat_axis=0, tiled=True)
        arrived = arrived.reshape(band_count, 2, blk, col_width)
        first, second = arrived[:, 0], arrived[:, 1]
        density = jnp.einsum("sic,sjc->ij", first, second, precision=PRECISION)
        kernel = density * coulomb[slot]
        onto_first = jnp.einsum("ij,sjc->sic", kernel, second, precision=PRECISION)
        onto_second = jnp.einsum("ij,sic->sjc", kernel, first, precision=PRECISION)
        scale = jnp.where(own_pairs[2 * slot] == own_pairs[2 * slot + 1], 0.5, 1.0)
        outbound = jnp.stack([onto_first, onto_second], axis=1) * scale
        returned = lax.all_to_all(outbound, "band", split_axis=0, concat_axis=0, tiled=True)
        returned = returned.reshape(band_count, 2, group_count, band_count, piece_rows, col_width)
        part = jnp.einsum("sqk,sqgjpc->gjkpc", pick, returned, precision=EXACT)
        summed = part if summed is None else summed + part
    parts = lax.all_to_all(summed, "grp", split_axis=0, concat_axis=0, tiled=True)
    mine = parts.sum(axis=0)
    return mine.reshape(band_count * block_count * piece_rows, col_width)


def solution(mesh):
    placed = (P("grp", "band"), P(), P(("grp", "band"), None, None))
    return jax.shard_map(
        body, mesh=mesh, in_specs=placed, out_specs=P("grp", "band"), check_vma=False
    )
```

```python
import jax
import jax.numpy as jnp
from jax import lax
from jax.sharding import PartitionSpec as P

PRECISION = lax.Precision.HIGH


def slot_work(first_block, second_block, coulomb_tile, diagonal):
    density = jnp.dot(
        first_block, second_block.T, precision=PRECISION, preferred_element_type=jnp.float32
    )
    kernel = density * coulomb_tile
    onto_first = jnp.dot(kernel, second_block, precision=PRECISION, preferred_element_type=jnp.float32)
    onto_second = jnp.dot(kernel.T, first_block, precision=PRECISION, preferred_element_type=jnp.float32)
    scale = jnp.where(diagonal, 0.5, 1.0)
    return jnp.stack([onto_first, onto_second], 0) * scale


def body(orbitals, requests, coulomb):
    group_count = lax.axis_size("grp")
    band_count = lax.axis_size("band")
    devices = group_count * band_count
    blk = coulomb.shape[1]
    col_width = orbitals.shape[1]
    orbital_width = col_width * band_count
    piece_rows = blk // devices
    slot_count = coulomb.shape[0]
    copies = jnp.broadcast_to(orbitals[None], (group_count,) + orbitals.shape)
    all_points = lax.all_to_all(copies, "grp", split_axis=0, concat_axis=0, tiled=True)
    block_count = all_points.shape[0] * all_points.shape[1] // (devices * piece_rows)
    blocks = (
        all_points.reshape(devices, block_count, piece_rows, col_width)
        .transpose(1, 0, 2, 3)
        .reshape(block_count, blk, col_width)
    )
    group_index = lax.axis_index("grp")
    band_index = lax.axis_index("band")
    group_requests = lax.dynamic_slice_in_dim(requests, group_index * band_count, band_count, 0)
    live = (group_requests >= 0).astype(jnp.float32)
    own_pairs = lax.dynamic_index_in_dim(group_requests, band_index, 0, keepdims=False)
    returned = []
    for slot in range(slot_count):
        wanted = group_requests[:, 2 * slot : 2 * slot + 2]
        outgoing = jnp.take(blocks, jnp.maximum(wanted, 0), axis=0)
        outgoing = outgoing * live[:, 2 * slot : 2 * slot + 2, None, None]
        arrived = lax.all_to_all(outgoing, "band", split_axis=0, concat_axis=0, tiled=True)
        pair_rows = arrived.transpose(1, 2, 0, 3).reshape(2, blk, orbital_width)
        diagonal = own_pairs[2 * slot] == own_pairs[2 * slot + 1]
        result = slot_work(pair_rows[0], pair_rows[1], coulomb[slot], diagonal)
        outbound = result.reshape(2, blk, band_count, col_width).transpose(2, 0, 1, 3)
        returned.append(lax.all_to_all(outbound, "band", split_axis=0, concat_axis=0, tiled=True))
    returned = jnp.concatenate(returned, axis=1)
    one_hot = (
        group_requests[:, :, None] == jnp.arange(block_count, dtype=jnp.int32)[None, None, :]
    ).astype(jnp.float32)
    summed = jnp.einsum("srk,srpc->kpc", one_hot, returned, precision=lax.Precision.HIGHEST)
    summed = summed.reshape(block_count, group_count, band_count, piece_rows, col_width)
    summed = summed.transpose(1, 0, 2, 3, 4)
    parts = lax.all_to_all(summed, "grp", split_axis=0, concat_axis=0, tiled=True)
    mine = parts.sum(axis=0).transpose(1, 0, 2, 3)
    return mine.reshape(band_count * block_count * piece_rows, col_width)


def solution(mesh):
    placed = (P("grp", "band"), P(), P(("grp", "band"), None, None))
    return jax.shard_map(
        body, mesh=mesh, in_specs=placed, out_specs=P("grp", "band"), check_vma=False
    )
```

```python
import jax
import jax.numpy as jnp
from jax import lax
from jax.sharding import PartitionSpec as P

PRECISION = lax.Precision.HIGH


def slot_work(first_block, second_block, coulomb_tile, diagonal):
    density = jnp.dot(
        first_block, second_block.T, precision=PRECISION, preferred_element_type=jnp.float32
    )
    kernel = density * coulomb_tile
    onto_first = jnp.dot(kernel, second_block, precision=PRECISION, preferred_element_type=jnp.float32)
    onto_second = jnp.dot(kernel.T, first_block, precision=PRECISION, preferred_element_type=jnp.float32)
    scale = jnp.where(diagonal, 0.5, 1.0)
    return jnp.stack([onto_first, onto_second], 0) * scale


def line_gather(x, axis, count):
    index = lax.axis_index(axis)
    spare = jnp.zeros((count + 1,) + x.shape, x.dtype)
    spare = lax.dynamic_update_index_in_dim(spare, x, index, 0)
    rightward, leftward = x, x
    for step in range(1, count):
        rightward = lax.ppermute(rightward, axis, [(i, i + 1) for i in range(step - 1, count - 1)])
        leftward = lax.ppermute(leftward, axis, [(i + 1, i) for i in range(0, count - step)])
        from_left = jnp.where(index >= step, index - step, count)
        from_right = jnp.where(index + step < count, index + step, count)
        spare = lax.dynamic_update_index_in_dim(spare, rightward, from_left, 0)
        spare = lax.dynamic_update_index_in_dim(spare, leftward, from_right, 0)
    return spare[:count]


def line_reduce(parts, axis, count):
    index = lax.axis_index(axis)

    def part_for(target):
        return lax.dynamic_index_in_dim(parts, jnp.clip(target, 0, count - 1), 0, keepdims=False)

    rightward = jnp.zeros(parts.shape[1:], parts.dtype)
    leftward = jnp.zeros(parts.shape[1:], parts.dtype)
    for step in range(1, count):
        send_right = rightward + part_for(index + count - step)
        send_left = leftward + part_for(index - count + step)
        rightward = lax.ppermute(send_right, axis, [(i, i + 1) for i in range(0, step)])
        leftward = lax.ppermute(send_left, axis, [(i, i - 1) for i in range(count - step, count)])
    return part_for(index) + rightward + leftward


def body(orbitals, requests, coulomb):
    group_count = lax.axis_size("grp")
    band_count = lax.axis_size("band")
    devices = group_count * band_count
    blk = coulomb.shape[1]
    col_width = orbitals.shape[1]
    orbital_width = col_width * band_count
    piece_rows = blk // devices
    slot_count = coulomb.shape[0]
    all_points = line_gather(orbitals, "grp", group_count)
    block_count = all_points.shape[0] * all_points.shape[1] // (devices * piece_rows)
    blocks = (
        all_points.reshape(devices, block_count, piece_rows, col_width)
        .transpose(1, 0, 2, 3)
        .reshape(block_count, blk, col_width)
    )
    group_index = lax.axis_index("grp")
    band_index = lax.axis_index("band")
    group_requests = lax.dynamic_slice_in_dim(requests, group_index * band_count, band_count, 0)
    live = (group_requests >= 0).astype(jnp.float32)
    own_pairs = lax.dynamic_index_in_dim(group_requests, band_index, 0, keepdims=False)
    returned = []
    for slot in range(slot_count):
        wanted = group_requests[:, 2 * slot : 2 * slot + 2]
        outgoing = jnp.take(blocks, jnp.maximum(wanted, 0), axis=0)
        outgoing = outgoing * live[:, 2 * slot : 2 * slot + 2, None, None]
        arrived = lax.all_to_all(outgoing, "band", split_axis=0, concat_axis=0, tiled=True)
        pair_rows = arrived.transpose(1, 2, 0, 3).reshape(2, blk, orbital_width)
        diagonal = own_pairs[2 * slot] == own_pairs[2 * slot + 1]
        result = slot_work(pair_rows[0], pair_rows[1], coulomb[slot], diagonal)
        outbound = result.reshape(2, blk, band_count, col_width).transpose(2, 0, 1, 3)
        returned.append(lax.all_to_all(outbound, "band", split_axis=0, concat_axis=0, tiled=True))
    returned = jnp.concatenate(returned, axis=1)
    one_hot = (
        group_requests[:, :, None] == jnp.arange(block_count, dtype=jnp.int32)[None, None, :]
    ).astype(jnp.float32)
    summed = jnp.einsum("srk,srpc->kpc", one_hot, returned, precision=lax.Precision.HIGHEST)
    summed = summed.reshape(block_count, group_count, band_count, piece_rows, col_width)
    summed = summed.transpose(1, 0, 2, 3, 4)
    mine = line_reduce(summed, "grp", group_count).transpose(1, 0, 2, 3)
    return mine.reshape(band_count * block_count * piece_rows, col_width)


def solution(mesh):
    placed = (P("grp", "band"), P(), P(("grp", "band"), None, None))
    return jax.shard_map(
        body, mesh=mesh, in_specs=placed, out_specs=P("grp", "band"), check_vma=False
    )
```

```python
import jax
import jax.numpy as jnp
from jax import lax
from jax.sharding import PartitionSpec as P

PRECISION = lax.Precision.HIGH


def slot_work(first_block, second_block, coulomb_tile, diagonal):
    density = jnp.dot(
        first_block, second_block.T, precision=PRECISION, preferred_element_type=jnp.float32
    )
    kernel = density * coulomb_tile
    onto_first = jnp.dot(kernel, second_block, precision=PRECISION, preferred_element_type=jnp.float32)
    onto_second = jnp.dot(kernel.T, first_block, precision=PRECISION, preferred_element_type=jnp.float32)
    scale = jnp.where(diagonal, 0.5, 1.0)
    return jnp.stack([onto_first, onto_second], 0) * scale


def line_gather(x, axis, count):
    index = lax.axis_index(axis)
    spare = jnp.zeros((count + 1,) + x.shape, x.dtype)
    spare = lax.dynamic_update_index_in_dim(spare, x, index, 0)
    rightward, leftward = x, x
    for step in range(1, count):
        rightward = lax.ppermute(rightward, axis, [(i, i + 1) for i in range(step - 1, count - 1)])
        leftward = lax.ppermute(leftward, axis, [(i + 1, i) for i in range(0, count - step)])
        from_left = jnp.where(index >= step, index - step, count)
        from_right = jnp.where(index + step < count, index + step, count)
        spare = lax.dynamic_update_index_in_dim(spare, rightward, from_left, 0)
        spare = lax.dynamic_update_index_in_dim(spare, leftward, from_right, 0)
    return spare[:count]


def line_reduce(parts, axis, count):
    index = lax.axis_index(axis)

    def part_for(target):
        return lax.dynamic_index_in_dim(parts, jnp.clip(target, 0, count - 1), 0, keepdims=False)

    rightward = jnp.zeros(parts.shape[1:], parts.dtype)
    leftward = jnp.zeros(parts.shape[1:], parts.dtype)
    for step in range(1, count):
        send_right = rightward + part_for(index + count - step)
        send_left = leftward + part_for(index - count + step)
        rightward = lax.ppermute(send_right, axis, [(i, i + 1) for i in range(0, step)])
        leftward = lax.ppermute(send_left, axis, [(i, i - 1) for i in range(count - step, count)])
    return part_for(index) + rightward + leftward


def body(orbitals, requests, coulomb):
    group_count = lax.axis_size("grp")
    band_count = lax.axis_size("band")
    devices = group_count * band_count
    blk = coulomb.shape[1]
    orbital_width = orbitals.shape[1] * band_count
    piece_rows = blk // devices
    slot_count = coulomb.shape[0]
    block_count = orbitals.shape[0] // (band_count * piece_rows)
    own_rows = lax.all_to_all(orbitals, "band", split_axis=0, concat_axis=1, tiled=True)
    pieces = line_gather(own_rows, "grp", group_count)
    pieces = pieces.reshape(group_count, block_count, piece_rows, orbital_width)
    group_index = lax.axis_index("grp")
    band_index = lax.axis_index("band")
    group_requests = lax.dynamic_slice_in_dim(requests, group_index * band_count, band_count, 0)
    live = (group_requests >= 0).astype(jnp.float32)
    own_pairs = lax.dynamic_index_in_dim(group_requests, band_index, 0, keepdims=False)
    returned = []
    for slot in range(slot_count):
        wanted = group_requests[:, 2 * slot : 2 * slot + 2]
        outgoing = jnp.take(pieces, jnp.maximum(wanted, 0), axis=1)
        outgoing = outgoing * live[None, :, 2 * slot : 2 * slot + 2, None, None]
        outgoing = outgoing.transpose(1, 2, 0, 3, 4)
        arrived = lax.all_to_all(outgoing, "band", split_axis=0, concat_axis=0, tiled=True)
        pair_rows = arrived.transpose(1, 2, 0, 3, 4).reshape(2, blk, orbital_width)
        diagonal = own_pairs[2 * slot] == own_pairs[2 * slot + 1]
        result = slot_work(pair_rows[0], pair_rows[1], coulomb[slot], diagonal)
        outbound = result.reshape(2, group_count, band_count, piece_rows, orbital_width)
        outbound = outbound.transpose(2, 0, 1, 3, 4)
        returned.append(lax.all_to_all(outbound, "band", split_axis=0, concat_axis=0, tiled=True))
    returned = jnp.concatenate(returned, axis=1)
    one_hot = (
        group_requests[:, :, None] == jnp.arange(block_count, dtype=jnp.int32)[None, None, :]
    ).astype(jnp.float32)
    summed = jnp.einsum("srk,srgpn->gkpn", one_hot, returned, precision=lax.Precision.HIGHEST)
    parts = lax.all_to_all(summed, "grp", split_axis=0, concat_axis=0, tiled=True)
    home_rows = parts.sum(axis=0).reshape(block_count * piece_rows, orbital_width)
    return lax.all_to_all(home_rows, "band", split_axis=1, concat_axis=0, tiled=True)


def solution(mesh):
    placed = (P("grp", "band"), P(), P(("grp", "band"), None, None))
    return jax.shard_map(
        body, mesh=mesh, in_specs=placed, out_specs=P("grp", "band"), check_vma=False
    )
```

```python
import jax
import jax.numpy as jnp
from jax import lax
from jax.sharding import PartitionSpec as P

PRECISION = lax.Precision.HIGH


def slot_work(first_block, second_block, coulomb_tile, diagonal):
    density = jnp.dot(
        first_block, second_block.T, precision=PRECISION, preferred_element_type=jnp.float32
    )
    kernel = density * coulomb_tile
    onto_first = jnp.dot(kernel, second_block, precision=PRECISION, preferred_element_type=jnp.float32)
    onto_second = jnp.dot(kernel.T, first_block, precision=PRECISION, preferred_element_type=jnp.float32)
    scale = jnp.where(diagonal, 0.5, 1.0)
    return jnp.stack([onto_first, onto_second], 0) * scale


def line_gather(x, axis, count):
    index = lax.axis_index(axis)
    spare = jnp.zeros((count + 1,) + x.shape, x.dtype)
    spare = lax.dynamic_update_index_in_dim(spare, x, index, 0)
    rightward, leftward = x, x
    for step in range(1, count):
        rightward = lax.ppermute(rightward, axis, [(i, i + 1) for i in range(step - 1, count - 1)])
        leftward = lax.ppermute(leftward, axis, [(i + 1, i) for i in range(0, count - step)])
        from_left = jnp.where(index >= step, index - step, count)
        from_right = jnp.where(index + step < count, index + step, count)
        spare = lax.dynamic_update_index_in_dim(spare, rightward, from_left, 0)
        spare = lax.dynamic_update_index_in_dim(spare, leftward, from_right, 0)
    return spare[:count]


def line_reduce(parts, axis, count):
    index = lax.axis_index(axis)

    def part_for(target):
        return lax.dynamic_index_in_dim(parts, jnp.clip(target, 0, count - 1), 0, keepdims=False)

    rightward = jnp.zeros(parts.shape[1:], parts.dtype)
    leftward = jnp.zeros(parts.shape[1:], parts.dtype)
    for step in range(1, count):
        send_right = rightward + part_for(index + count - step)
        send_left = leftward + part_for(index - count + step)
        rightward = lax.ppermute(send_right, axis, [(i, i + 1) for i in range(0, step)])
        leftward = lax.ppermute(send_left, axis, [(i, i - 1) for i in range(count - step, count)])
    return part_for(index) + rightward + leftward


def body(orbitals, requests, coulomb):
    group_count = lax.axis_size("grp")
    band_count = lax.axis_size("band")
    devices = group_count * band_count
    blk = coulomb.shape[1]
    orbital_width = orbitals.shape[1] * band_count
    piece_rows = blk // devices
    slot_count = coulomb.shape[0]
    block_count = orbitals.shape[0] // (band_count * piece_rows)
    own_rows = lax.all_to_all(orbitals, "band", split_axis=0, concat_axis=1, tiled=True)
    pieces = line_gather(own_rows, "grp", group_count)
    pieces = pieces.reshape(group_count, block_count, piece_rows, orbital_width)
    group_index = lax.axis_index("grp")
    band_index = lax.axis_index("band")
    group_requests = lax.dynamic_slice_in_dim(requests, group_index * band_count, band_count, 0)
    live = (group_requests >= 0).astype(jnp.float32)
    own_pairs = lax.dynamic_index_in_dim(group_requests, band_index, 0, keepdims=False)
    returned = []
    for slot in range(slot_count):
        wanted = group_requests[:, 2 * slot : 2 * slot + 2]
        outgoing = jnp.take(pieces, jnp.maximum(wanted, 0), axis=1)
        outgoing = outgoing * live[None, :, 2 * slot : 2 * slot + 2, None, None]
        outgoing = outgoing.transpose(1, 2, 0, 3, 4)
        arrived = lax.all_to_all(outgoing, "band", split_axis=0, concat_axis=0, tiled=True)
        pair_rows = arrived.transpose(1, 2, 0, 3, 4).reshape(2, blk, orbital_width)
        diagonal = own_pairs[2 * slot] == own_pairs[2 * slot + 1]
        result = slot_work(pair_rows[0], pair_rows[1], coulomb[slot], diagonal)
        outbound = result.reshape(2, group_count, band_count, piece_rows, orbital_width)
        outbound = outbound.transpose(2, 0, 1, 3, 4)
        returned.append(lax.all_to_all(outbound, "band", split_axis=0, concat_axis=0, tiled=True))
    returned = jnp.concatenate(returned, axis=1)
    one_hot = (
        group_requests[:, :, None] == jnp.arange(block_count, dtype=jnp.int32)[None, None, :]
    ).astype(jnp.float32)
    summed = jnp.einsum("srk,srgpn->gkpn", one_hot, returned, precision=lax.Precision.HIGHEST)
    home_rows = line_reduce(summed, "grp", group_count).reshape(block_count * piece_rows, orbital_width)
    return lax.all_to_all(home_rows, "band", split_axis=1, concat_axis=0, tiled=True)


def solution(mesh):
    placed = (P("grp", "band"), P(), P(("grp", "band"), None, None))
    return jax.shard_map(
        body, mesh=mesh, in_specs=placed, out_specs=P("grp", "band"), check_vma=False
    )
```

```python
import jax
import jax.numpy as jnp
from jax import lax
from jax.sharding import PartitionSpec as P

PRECISION = lax.Precision.HIGH


def band_exchange(outgoing):
    return lax.all_to_all(outgoing, "band", split_axis=0, concat_axis=0, tiled=True)


def line_gather(x, axis, count, riders=()):
    index = lax.axis_index(axis)
    spare = jnp.zeros((count + 1,) + x.shape, x.dtype)
    spare = lax.dynamic_update_index_in_dim(spare, x, index, 0)
    rightward, leftward = x, x
    carried = []
    for step in range(1, count):
        rider = step - 1 < len(riders)
        if rider:
            rightward, leftward, load = lax.optimization_barrier((rightward, leftward, riders[step - 1]))
        rightward = lax.ppermute(rightward, axis, [(i, i + 1) for i in range(step - 1, count - 1)])
        leftward = lax.ppermute(leftward, axis, [(i + 1, i) for i in range(0, count - step)])
        if rider:
            rightward, leftward, load = lax.optimization_barrier((rightward, leftward, band_exchange(load)))
            carried.append(load)
        from_left = jnp.where(index >= step, index - step, count)
        from_right = jnp.where(index + step < count, index + step, count)
        spare = lax.dynamic_update_index_in_dim(spare, rightward, from_left, 0)
        spare = lax.dynamic_update_index_in_dim(spare, leftward, from_right, 0)
    carried += [band_exchange(load) for load in riders[len(carried):]]
    return spare[:count], carried


def line_reduce(parts, axis, count, riders=()):
    index = lax.axis_index(axis)

    def part_for(target):
        return lax.dynamic_index_in_dim(parts, jnp.clip(target, 0, count - 1), 0, keepdims=False)

    rightward = jnp.zeros(parts.shape[1:], parts.dtype)
    leftward = jnp.zeros(parts.shape[1:], parts.dtype)
    carried = []
    for step in range(1, count):
        send_right = rightward + part_for(index + count - step)
        send_left = leftward + part_for(index - count + step)
        rider = step - 1 < len(riders)
        if rider:
            send_right, send_left, load = lax.optimization_barrier((send_right, send_left, riders[step - 1]))
        rightward = lax.ppermute(send_right, axis, [(i, i + 1) for i in range(0, step)])
        leftward = lax.ppermute(send_left, axis, [(i, i - 1) for i in range(count - step, count)])
        if rider:
            rightward, leftward, load = lax.optimization_barrier((rightward, leftward, band_exchange(load)))
            carried.append(load)
    carried += [band_exchange(load) for load in riders[len(carried):]]
    return part_for(index) + rightward + leftward, carried


def body(orbitals, requests, coulomb):
    group_count = lax.axis_size("grp")
    band_count = lax.axis_size("band")
    devices = group_count * band_count
    blk = coulomb.shape[1]
    orbital_width = orbitals.shape[1] * band_count
    half = orbital_width // 2
    piece_rows = blk // devices
    slot_count = coulomb.shape[0]
    block_count = orbitals.shape[0] // (band_count * piece_rows)
    own_rows = lax.all_to_all(orbitals, "band", split_axis=0, concat_axis=1, tiled=True)
    group_index = lax.axis_index("grp")
    band_index = lax.axis_index("band")
    group_requests = lax.dynamic_slice_in_dim(requests, group_index * band_count, band_count, 0)
    live = (group_requests >= 0).astype(jnp.float32)
    own_pairs = lax.dynamic_index_in_dim(group_requests, band_index, 0, keepdims=False)
    one_hot = (
        group_requests[:, :, None] == jnp.arange(block_count, dtype=jnp.int32)[None, None, :]
    ).astype(jnp.float32)

    def requested(pieces, slot):
        wanted = group_requests[:, 2 * slot : 2 * slot + 2]
        mask = live[None, :, 2 * slot : 2 * slot + 2, None, None]
        outgoing = jnp.take(pieces, jnp.maximum(wanted, 0), axis=1) * mask
        return outgoing.transpose(1, 2, 0, 3, 4)

    def shape_pieces(gathered):
        return gathered.reshape(group_count, block_count, piece_rows, half)

    first_pieces = shape_pieces(line_gather(own_rows[:, :half], "grp", group_count)[0])
    first_loads = [requested(first_pieces, slot) for slot in range(slot_count)]
    second_pieces, first_arrived = line_gather(own_rows[:, half:], "grp", group_count, first_loads)
    second_pieces = shape_pieces(second_pieces)
    second_arrived = [band_exchange(requested(second_pieces, slot)) for slot in range(slot_count)]
    returned = [[], []]
    held = []
    for slot in range(slot_count):
        rows = [
            arrived.transpose(1, 2, 0, 3, 4).reshape(2, blk, half)
            for arrived in (first_arrived[slot], second_arrived[slot])
        ]
        density = sum(
            jnp.dot(r[0], r[1].T, precision=PRECISION, preferred_element_type=jnp.float32) for r in rows
        )
        kernel = density * coulomb[slot]
        scale = jnp.where(own_pairs[2 * slot] == own_pairs[2 * slot + 1], 0.5, 1.0)
        for h in range(2):
            onto_first = jnp.dot(kernel, rows[h][1], precision=PRECISION, preferred_element_type=jnp.float32)
            onto_second = jnp.dot(kernel.T, rows[h][0], precision=PRECISION, preferred_element_type=jnp.float32)
            outbound = (jnp.stack([onto_first, onto_second], 0) * scale).reshape(
                2, group_count, band_count, piece_rows, half
            )
            outbound = outbound.transpose(2, 0, 1, 3, 4)
            if h == 0:
                returned[0].append(band_exchange(outbound))
            else:
                held.append(outbound)

    def sum_blocks(returned):
        gathered = jnp.concatenate(returned, axis=1)
        return jnp.einsum("srk,srgpn->gkpn", one_hot, gathered, precision=lax.Precision.HIGHEST)

    first_home, second_returned = line_reduce(sum_blocks(returned[0]), "grp", group_count, held)
    second_home, _ = line_reduce(sum_blocks(second_returned), "grp", group_count)
    home_rows = jnp.concatenate([first_home, second_home], axis=-1).reshape(
        block_count * piece_rows, orbital_width
    )
    return lax.all_to_all(home_rows, "band", split_axis=1, concat_axis=0, tiled=True)


def solution(mesh):
    placed = (P("grp", "band"), P(), P(("grp", "band"), None, None))
    return jax.shard_map(
        body, mesh=mesh, in_specs=placed, out_specs=P("grp", "band"), check_vma=False
    )
```

```python
import jax
import jax.numpy as jnp
from jax import lax
from jax.sharding import PartitionSpec as P

PRECISION = lax.Precision.HIGH


def band_exchange(outgoing):
    return lax.all_to_all(outgoing, "band", split_axis=0, concat_axis=0, tiled=True)


def line_gather(x, axis, count, riders=()):
    index = lax.axis_index(axis)
    spare = jnp.zeros((count + 1,) + x.shape, x.dtype)
    spare = lax.dynamic_update_index_in_dim(spare, x, index, 0)
    rightward, leftward = x, x
    carried = []
    for step in range(1, count):
        rider = step - 1 < len(riders)
        if rider:
            rightward, leftward, load = lax.optimization_barrier((rightward, leftward, riders[step - 1]))
        rightward = lax.ppermute(rightward, axis, [(i, i + 1) for i in range(step - 1, count - 1)])
        leftward = lax.ppermute(leftward, axis, [(i + 1, i) for i in range(0, count - step)])
        if rider:
            rightward, leftward, load = lax.optimization_barrier((rightward, leftward, band_exchange(load)))
            carried.append(load)
        from_left = jnp.where(index >= step, index - step, count)
        from_right = jnp.where(index + step < count, index + step, count)
        spare = lax.dynamic_update_index_in_dim(spare, rightward, from_left, 0)
        spare = lax.dynamic_update_index_in_dim(spare, leftward, from_right, 0)
    carried += [band_exchange(load) for load in riders[len(carried):]]
    return spare[:count], carried


def line_reduce(parts, axis, count, riders=()):
    index = lax.axis_index(axis)

    def part_for(target):
        return lax.dynamic_index_in_dim(parts, jnp.clip(target, 0, count - 1), 0, keepdims=False)

    rightward = jnp.zeros(parts.shape[1:], parts.dtype)
    leftward = jnp.zeros(parts.shape[1:], parts.dtype)
    carried = []
    for step in range(1, count):
        send_right = rightward + part_for(index + count - step)
        send_left = leftward + part_for(index - count + step)
        rider = step - 1 < len(riders)
        if rider:
            send_right, send_left, load = lax.optimization_barrier((send_right, send_left, riders[step - 1]))
        rightward = lax.ppermute(send_right, axis, [(i, i + 1) for i in range(0, step)])
        leftward = lax.ppermute(send_left, axis, [(i, i - 1) for i in range(count - step, count)])
        if rider:
            rightward, leftward, load = lax.optimization_barrier((rightward, leftward, band_exchange(load)))
            carried.append(load)
    carried += [band_exchange(load) for load in riders[len(carried):]]
    return part_for(index) + rightward + leftward, carried


def body(orbitals, requests, coulomb):
    group_count = lax.axis_size("grp")
    band_count = lax.axis_size("band")
    devices = group_count * band_count
    blk = coulomb.shape[1]
    orbital_width = orbitals.shape[1] * band_count
    half = orbital_width // 2
    piece_rows = blk // devices
    slot_count = coulomb.shape[0]
    block_count = orbitals.shape[0] // (band_count * piece_rows)
    col_half = orbitals.shape[1] // 2
    own_rows = [
        lax.all_to_all(
            orbitals[:, h * col_half : (h + 1) * col_half], "band", split_axis=0, concat_axis=1, tiled=True
        )
        for h in range(2)
    ]
    group_index = lax.axis_index("grp")
    band_index = lax.axis_index("band")
    group_requests = lax.dynamic_slice_in_dim(requests, group_index * band_count, band_count, 0)
    live = (group_requests >= 0).astype(jnp.float32)
    own_pairs = lax.dynamic_index_in_dim(group_requests, band_index, 0, keepdims=False)
    one_hot = (
        group_requests[:, :, None] == jnp.arange(block_count, dtype=jnp.int32)[None, None, :]
    ).astype(jnp.float32)

    def requested(pieces, slot):
        wanted = group_requests[:, 2 * slot : 2 * slot + 2]
        mask = live[None, :, 2 * slot : 2 * slot + 2, None, None]
        outgoing = jnp.take(pieces, jnp.maximum(wanted, 0), axis=1) * mask
        return outgoing.transpose(1, 2, 0, 3, 4)

    def shape_pieces(gathered):
        return gathered.reshape(group_count, block_count, piece_rows, half)

    first_pieces = shape_pieces(line_gather(own_rows[0], "grp", group_count)[0])
    first_loads = [requested(first_pieces, slot) for slot in range(slot_count)]
    second_pieces, first_arrived = line_gather(own_rows[1], "grp", group_count, first_loads)
    second_pieces = shape_pieces(second_pieces)
    second_arrived = [band_exchange(requested(second_pieces, slot)) for slot in range(slot_count)]
    returned = [[], []]
    held = []
    for slot in range(slot_count):
        rows = [
            arrived.transpose(1, 2, 0, 3, 4).reshape(2, blk, half)
            for arrived in (first_arrived[slot], second_arrived[slot])
        ]
        density = sum(
            jnp.dot(r[0], r[1].T, precision=PRECISION, preferred_element_type=jnp.float32) for r in rows
        )
        kernel = density * coulomb[slot]
        scale = jnp.where(own_pairs[2 * slot] == own_pairs[2 * slot + 1], 0.5, 1.0)
        for h in range(2):
            onto_first = jnp.dot(kernel, rows[h][1], precision=PRECISION, preferred_element_type=jnp.float32)
            onto_second = jnp.dot(kernel.T, rows[h][0], precision=PRECISION, preferred_element_type=jnp.float32)
            outbound = (jnp.stack([onto_first, onto_second], 0) * scale).reshape(
                2, group_count, band_count, piece_rows, half
            )
            outbound = outbound.transpose(2, 0, 1, 3, 4)
            if h == 0:
                returned[0].append(band_exchange(outbound))
            else:
                held.append(outbound)

    def sum_blocks(returned):
        gathered = jnp.concatenate(returned, axis=1)
        return jnp.einsum("srk,srgpn->gkpn", one_hot, gathered, precision=lax.Precision.HIGHEST)

    first_home, second_returned = line_reduce(sum_blocks(returned[0]), "grp", group_count, held)
    second_home, _ = line_reduce(sum_blocks(second_returned), "grp", group_count)
    home = [
        lax.all_to_all(
            rows.reshape(block_count * piece_rows, half), "band", split_axis=1, concat_axis=0, tiled=True
        )
        for rows in (first_home, second_home)
    ]
    return jnp.concatenate(home, axis=1)


def solution(mesh):
    placed = (P("grp", "band"), P(), P(("grp", "band"), None, None))
    return jax.shard_map(
        body, mesh=mesh, in_specs=placed, out_specs=P("grp", "band"), check_vma=False
    )
```

```python
import jax
import jax.numpy as jnp
from jax import lax
from jax.sharding import PartitionSpec as P

PRECISION = lax.Precision.HIGH


def band_exchange(outgoing):
    return lax.all_to_all(outgoing, "band", split_axis=0, concat_axis=0, tiled=True)


def line_gather(x, axis, count, riders=()):
    index = lax.axis_index(axis)
    spare = jnp.zeros((count + 1,) + x.shape, x.dtype)
    spare = lax.dynamic_update_index_in_dim(spare, x, index, 0)
    rightward, leftward = x, x
    carried = []
    for step in range(1, count):
        rider = step - 1 < len(riders)
        if rider:
            rightward, leftward, load = lax.optimization_barrier((rightward, leftward, riders[step - 1]))
        rightward = lax.ppermute(rightward, axis, [(i, i + 1) for i in range(step - 1, count - 1)])
        leftward = lax.ppermute(leftward, axis, [(i + 1, i) for i in range(0, count - step)])
        if rider:
            rightward, leftward, load = lax.optimization_barrier((rightward, leftward, band_exchange(load)))
            carried.append(load)
        from_left = jnp.where(index >= step, index - step, count)
        from_right = jnp.where(index + step < count, index + step, count)
        spare = lax.dynamic_update_index_in_dim(spare, rightward, from_left, 0)
        spare = lax.dynamic_update_index_in_dim(spare, leftward, from_right, 0)
    carried += [band_exchange(load) for load in riders[len(carried):]]
    return spare[:count], carried


def line_reduce(parts, axis, count, riders=()):
    index = lax.axis_index(axis)

    def part_for(target):
        return lax.dynamic_index_in_dim(parts, jnp.clip(target, 0, count - 1), 0, keepdims=False)

    rightward = jnp.zeros(parts.shape[1:], parts.dtype)
    leftward = jnp.zeros(parts.shape[1:], parts.dtype)
    carried = []
    for step in range(1, count):
        send_right = rightward + part_for(index + count - step)
        send_left = leftward + part_for(index - count + step)
        rider = step - 1 < len(riders)
        if rider:
            send_right, send_left, load = lax.optimization_barrier((send_right, send_left, riders[step - 1]))
        rightward = lax.ppermute(send_right, axis, [(i, i + 1) for i in range(0, step)])
        leftward = lax.ppermute(send_left, axis, [(i, i - 1) for i in range(count - step, count)])
        if rider:
            rightward, leftward, load = lax.optimization_barrier((rightward, leftward, band_exchange(load)))
            carried.append(load)
    carried += [band_exchange(load) for load in riders[len(carried):]]
    return part_for(index) + rightward + leftward, carried


def body(orbitals, requests, coulomb):
    group_count = lax.axis_size("grp")
    band_count = lax.axis_size("band")
    devices = group_count * band_count
    blk = coulomb.shape[1]
    orbital_width = orbitals.shape[1] * band_count
    half = orbital_width // 2
    piece_rows = blk // devices
    slot_count = coulomb.shape[0]
    block_count = orbitals.shape[0] // (band_count * piece_rows)
    col_half = orbitals.shape[1] // 2
    own_rows = [
        lax.all_to_all(
            orbitals[:, h * col_half : (h + 1) * col_half], "band", split_axis=0, concat_axis=1, tiled=True
        )
        for h in range(2)
    ]
    group_index = lax.axis_index("grp")
    band_index = lax.axis_index("band")
    group_requests = lax.dynamic_slice_in_dim(requests, group_index * band_count, band_count, 0)
    live = (group_requests >= 0).astype(jnp.float32)
    own_pairs = lax.dynamic_index_in_dim(group_requests, band_index, 0, keepdims=False)
    one_hot = (
        group_requests[:, :, None] == jnp.arange(block_count, dtype=jnp.int32)[None, None, :]
    ).astype(jnp.float32)

    def requested(pieces, slot):
        wanted = group_requests[:, 2 * slot : 2 * slot + 2]
        mask = live[None, :, 2 * slot : 2 * slot + 2, None, None]
        outgoing = jnp.take(pieces, jnp.maximum(wanted, 0), axis=1) * mask
        return outgoing.transpose(1, 2, 0, 3, 4)

    def shape_pieces(gathered):
        return gathered.reshape(group_count, block_count, piece_rows, half)

    first_pieces = shape_pieces(line_gather(own_rows[0], "grp", group_count)[0])
    first_loads = [requested(first_pieces, slot) for slot in range(slot_count)]
    second_pieces, first_arrived = line_gather(own_rows[1], "grp", group_count, first_loads)
    second_pieces = shape_pieces(second_pieces)
    second_loads = [requested(second_pieces, slot) for slot in range(slot_count)]
    second_arrived = [band_exchange(load) for load in second_loads[:2]]
    returned = [[], []]
    held = []
    waiting = []
    for slot in range(slot_count):
        rows = [
            arrived.transpose(1, 2, 0, 3, 4).reshape(2, blk, half)
            for arrived in (first_arrived[slot], second_arrived[slot])
        ]
        density = sum(
            jnp.dot(r[0], r[1].T, precision=PRECISION, preferred_element_type=jnp.float32) for r in rows
        )
        kernel = density * coulomb[slot]
        scale = jnp.where(own_pairs[2 * slot] == own_pairs[2 * slot + 1], 0.5, 1.0)
        outbound = []
        for h in range(2):
            onto_first = jnp.dot(kernel, rows[h][1], precision=PRECISION, preferred_element_type=jnp.float32)
            onto_second = jnp.dot(kernel.T, rows[h][0], precision=PRECISION, preferred_element_type=jnp.float32)
            terms = (jnp.stack([onto_first, onto_second], 0) * scale).reshape(
                2, group_count, band_count, piece_rows, half
            )
            outbound.append(terms.transpose(2, 0, 1, 3, 4))
        held.append(outbound[1])
        if slot + 2 < slot_count:
            load, outbound[0] = lax.optimization_barrier((second_loads[slot + 2], outbound[0]))
            second_arrived.append(band_exchange(load))
        if waiting:
            waiting[0], outbound[0] = lax.optimization_barrier((waiting[0], outbound[0]))
            returned[0].append(band_exchange(waiting.pop()))
        waiting.append(outbound[0])
    returned[0].append(band_exchange(waiting.pop()))

    def sum_blocks(returned):
        gathered = jnp.concatenate(returned, axis=1)
        return jnp.einsum("srk,srgpn->gkpn", one_hot, gathered, precision=lax.Precision.HIGHEST)

    first_home, second_returned = line_reduce(sum_blocks(returned[0]), "grp", group_count, held)
    second_home, _ = line_reduce(sum_blocks(second_returned), "grp", group_count)
    home = [
        lax.all_to_all(
            rows.reshape(block_count * piece_rows, half), "band", split_axis=1, concat_axis=0, tiled=True
        )
        for rows in (first_home, second_home)
    ]
    return jnp.concatenate(home, axis=1)


def solution(mesh):
    placed = (P("grp", "band"), P(), P(("grp", "band"), None, None))
    return jax.shard_map(
        body, mesh=mesh, in_specs=placed, out_specs=P("grp", "band"), check_vma=False
    )
```

```python
import jax
import jax.numpy as jnp
from jax import lax
from jax.sharding import PartitionSpec as P

PRECISION = lax.Precision.HIGH


def band_exchange(outgoing):
    return lax.all_to_all(outgoing, "band", split_axis=0, concat_axis=0, tiled=True)


def line_gather(x, axis, count, riders=()):
    index = lax.axis_index(axis)
    spare = jnp.zeros((count + 1,) + x.shape, x.dtype)
    spare = lax.dynamic_update_index_in_dim(spare, x, index, 0)
    rightward, leftward = x, x
    carried = []
    for step in range(1, count):
        rider = step - 1 < len(riders)
        if rider:
            rightward, leftward, load = lax.optimization_barrier((rightward, leftward, riders[step - 1]))
        rightward = lax.ppermute(rightward, axis, [(i, i + 1) for i in range(step - 1, count - 1)])
        leftward = lax.ppermute(leftward, axis, [(i + 1, i) for i in range(0, count - step)])
        if rider:
            rightward, leftward, load = lax.optimization_barrier((rightward, leftward, band_exchange(load)))
            carried.append(load)
        from_left = jnp.where(index >= step, index - step, count)
        from_right = jnp.where(index + step < count, index + step, count)
        spare = lax.dynamic_update_index_in_dim(spare, rightward, from_left, 0)
        spare = lax.dynamic_update_index_in_dim(spare, leftward, from_right, 0)
    carried += [band_exchange(load) for load in riders[len(carried):]]
    return spare[:count], carried


def line_reduce(parts, axis, count, riders=(), exchange=band_exchange):
    index = lax.axis_index(axis)

    def part_for(target):
        return lax.dynamic_index_in_dim(parts, jnp.clip(target, 0, count - 1), 0, keepdims=False)

    rightward = jnp.zeros(parts.shape[1:], parts.dtype)
    leftward = jnp.zeros(parts.shape[1:], parts.dtype)
    carried = []
    for step in range(1, count):
        send_right = rightward + part_for(index + count - step)
        send_left = leftward + part_for(index - count + step)
        rider = step - 1 < len(riders)
        if rider:
            send_right, send_left, load = lax.optimization_barrier((send_right, send_left, riders[step - 1]))
        rightward = lax.ppermute(send_right, axis, [(i, i + 1) for i in range(0, step)])
        leftward = lax.ppermute(send_left, axis, [(i, i - 1) for i in range(count - step, count)])
        if rider:
            rightward, leftward, load = lax.optimization_barrier((rightward, leftward, exchange(load)))
            carried.append(load)
    carried += [exchange(load) for load in riders[len(carried):]]
    return part_for(index) + rightward + leftward, carried


def body(orbitals, requests, coulomb):
    group_count = lax.axis_size("grp")
    band_count = lax.axis_size("band")
    devices = group_count * band_count
    blk = coulomb.shape[1]
    orbital_width = orbitals.shape[1] * band_count
    half = orbital_width // 2
    piece_rows = blk // devices
    slot_count = coulomb.shape[0]
    block_count = orbitals.shape[0] // (band_count * piece_rows)
    col_half = orbitals.shape[1] // 2
    own_rows = [
        lax.all_to_all(
            orbitals[:, h * col_half : (h + 1) * col_half], "band", split_axis=0, concat_axis=1, tiled=True
        )
        for h in range(2)
    ]
    group_index = lax.axis_index("grp")
    band_index = lax.axis_index("band")
    group_requests = lax.dynamic_slice_in_dim(requests, group_index * band_count, band_count, 0)
    live = (group_requests >= 0).astype(jnp.float32)
    own_pairs = lax.dynamic_index_in_dim(group_requests, band_index, 0, keepdims=False)
    one_hot = (
        group_requests[:, :, None] == jnp.arange(block_count, dtype=jnp.int32)[None, None, :]
    ).astype(jnp.float32)

    def requested(pieces, slot):
        wanted = group_requests[:, 2 * slot : 2 * slot + 2]
        mask = live[None, :, 2 * slot : 2 * slot + 2, None, None]
        outgoing = jnp.take(pieces, jnp.maximum(wanted, 0), axis=1) * mask
        return outgoing.transpose(1, 2, 0, 3, 4)

    def shape_pieces(gathered):
        return gathered.reshape(group_count, block_count, piece_rows, half)

    first_pieces = shape_pieces(line_gather(own_rows[0], "grp", group_count)[0])
    first_loads = [requested(first_pieces, slot) for slot in range(slot_count)]
    second_pieces, first_arrived = line_gather(own_rows[1], "grp", group_count, first_loads)
    second_pieces = shape_pieces(second_pieces)
    second_arrived = [band_exchange(requested(second_pieces, slot)) for slot in range(slot_count)]
    returned = [[], []]
    held = []
    for slot in range(slot_count):
        rows = [
            arrived.transpose(1, 2, 0, 3, 4).reshape(2, blk, half)
            for arrived in (first_arrived[slot], second_arrived[slot])
        ]
        density = sum(
            jnp.dot(r[0], r[1].T, precision=PRECISION, preferred_element_type=jnp.float32) for r in rows
        )
        kernel = density * coulomb[slot]
        scale = jnp.where(own_pairs[2 * slot] == own_pairs[2 * slot + 1], 0.5, 1.0)
        for h in range(2):
            onto_first = jnp.dot(kernel, rows[h][1], precision=PRECISION, preferred_element_type=jnp.float32)
            onto_second = jnp.dot(kernel.T, rows[h][0], precision=PRECISION, preferred_element_type=jnp.float32)
            outbound = (jnp.stack([onto_first, onto_second], 0) * scale).reshape(
                2, group_count, band_count, piece_rows, half
            )
            outbound = outbound.transpose(2, 0, 1, 3, 4)
            if h == 0:
                returned[0].append(band_exchange(outbound))
            else:
                held.append(outbound)

    def sum_blocks(returned):
        gathered = jnp.concatenate(returned, axis=1)
        return jnp.einsum("srk,srgpn->gkpn", one_hot, gathered, precision=lax.Precision.HIGHEST)

    first_home, second_returned = line_reduce(sum_blocks(returned[0]), "grp", group_count, held)
    def home_rows(rows):
        rows = rows.reshape(block_count * piece_rows, half)
        return lax.all_to_all(rows, "band", split_axis=1, concat_axis=0, tiled=True)

    second_home, first_home = line_reduce(
        sum_blocks(second_returned), "grp", group_count, [first_home], home_rows
    )
    return jnp.concatenate([first_home[0], home_rows(second_home)], axis=1)


def solution(mesh):
    placed = (P("grp", "band"), P(), P(("grp", "band"), None, None))
    return jax.shard_map(
        body, mesh=mesh, in_specs=placed, out_specs=P("grp", "band"), check_vma=False
    )
```

```python
import jax
import jax.numpy as jnp
from jax import lax
from jax.sharding import PartitionSpec as P

PRECISION = lax.Precision.HIGH


def band_exchange(outgoing):
    return lax.all_to_all(outgoing, "band", split_axis=0, concat_axis=0, tiled=True)


def line_gather(x, axis, count, riders=()):
    index = lax.axis_index(axis)
    spare = jnp.zeros((count + 1,) + x.shape, x.dtype)
    spare = lax.dynamic_update_index_in_dim(spare, x, index, 0)
    rightward, leftward = x, x
    carried = []
    for step in range(1, count):
        rider = step - 1 < len(riders)
        if rider:
            rightward, leftward, load = lax.optimization_barrier((rightward, leftward, riders[step - 1]))
        rightward = lax.ppermute(rightward, axis, [(i, i + 1) for i in range(step - 1, count - 1)])
        leftward = lax.ppermute(leftward, axis, [(i + 1, i) for i in range(0, count - step)])
        if rider:
            rightward, leftward, load = lax.optimization_barrier((rightward, leftward, band_exchange(load)))
            carried.append(load)
        from_left = jnp.where(index >= step, index - step, count)
        from_right = jnp.where(index + step < count, index + step, count)
        spare = lax.dynamic_update_index_in_dim(spare, rightward, from_left, 0)
        spare = lax.dynamic_update_index_in_dim(spare, leftward, from_right, 0)
    carried += [band_exchange(load) for load in riders[len(carried):]]
    return spare[:count], carried


def line_reduce(parts, axis, count, riders=()):
    index = lax.axis_index(axis)

    def part_for(target):
        return lax.dynamic_index_in_dim(parts, jnp.clip(target, 0, count - 1), 0, keepdims=False)

    rightward = jnp.zeros(parts.shape[1:], parts.dtype)
    leftward = jnp.zeros(parts.shape[1:], parts.dtype)
    carried = []
    for step in range(1, count):
        send_right = rightward + part_for(index + count - step)
        send_left = leftward + part_for(index - count + step)
        rider = step - 1 < len(riders)
        if rider:
            send_right, send_left, load = lax.optimization_barrier((send_right, send_left, riders[step - 1]))
        rightward = lax.ppermute(send_right, axis, [(i, i + 1) for i in range(0, step)])
        leftward = lax.ppermute(send_left, axis, [(i, i - 1) for i in range(count - step, count)])
        if rider:
            rightward, leftward, load = lax.optimization_barrier((rightward, leftward, band_exchange(load)))
            carried.append(load)
    carried += [band_exchange(load) for load in riders[len(carried):]]
    return part_for(index) + rightward + leftward, carried


def body(orbitals, requests, coulomb):
    group_count = lax.axis_size("grp")
    band_count = lax.axis_size("band")
    devices = group_count * band_count
    blk = coulomb.shape[1]
    piece_rows = blk // devices
    slot_count = coulomb.shape[0]
    block_count = orbitals.shape[0] // (band_count * piece_rows)
    quarter = orbitals.shape[1] // 4
    bounds = [(0, quarter), (quarter, 3 * quarter), (3 * quarter, 4 * quarter)]
    own_rows = [
        lax.all_to_all(orbitals[:, lo:hi], "band", split_axis=0, concat_axis=1, tiled=True)
        for lo, hi in bounds
    ]
    group_index = lax.axis_index("grp")
    band_index = lax.axis_index("band")
    group_requests = lax.dynamic_slice_in_dim(requests, group_index * band_count, band_count, 0)
    live = (group_requests >= 0).astype(jnp.float32)
    own_pairs = lax.dynamic_index_in_dim(group_requests, band_index, 0, keepdims=False)
    one_hot = (
        group_requests[:, :, None] == jnp.arange(block_count, dtype=jnp.int32)[None, None, :]
    ).astype(jnp.float32)

    def requested(pieces, slot):
        wanted = group_requests[:, 2 * slot : 2 * slot + 2]
        mask = live[None, :, 2 * slot : 2 * slot + 2, None, None]
        outgoing = jnp.take(pieces, jnp.maximum(wanted, 0), axis=1) * mask
        return outgoing.transpose(1, 2, 0, 3, 4)

    def shape_pieces(gathered):
        return gathered.reshape(group_count, block_count, piece_rows, gathered.shape[-1])

    pieces = shape_pieces(line_gather(own_rows[0], "grp", group_count)[0])
    arrived = []
    for chunk in range(1, len(bounds)):
        loads = [requested(pieces, slot) for slot in range(slot_count)]
        gathered, carried = line_gather(own_rows[chunk], "grp", group_count, loads)
        arrived.append(carried)
        pieces = shape_pieces(gathered)
    arrived.append([band_exchange(requested(pieces, slot)) for slot in range(slot_count)])
    returned = [[] for _ in bounds]
    held = [[] for _ in bounds]
    for slot in range(slot_count):
        rows = [
            part[slot].transpose(1, 2, 0, 3, 4).reshape(2, blk, part[slot].shape[-1]) for part in arrived
        ]
        density = sum(
            jnp.dot(r[0], r[1].T, precision=PRECISION, preferred_element_type=jnp.float32) for r in rows
        )
        kernel = density * coulomb[slot]
        scale = jnp.where(own_pairs[2 * slot] == own_pairs[2 * slot + 1], 0.5, 1.0)
        for chunk, r in enumerate(rows):
            onto_first = jnp.dot(kernel, r[1], precision=PRECISION, preferred_element_type=jnp.float32)
            onto_second = jnp.dot(kernel.T, r[0], precision=PRECISION, preferred_element_type=jnp.float32)
            outbound = (jnp.stack([onto_first, onto_second], 0) * scale).reshape(
                2, group_count, band_count, piece_rows, r.shape[-1]
            )
            outbound = outbound.transpose(2, 0, 1, 3, 4)
            if chunk == 0:
                returned[0].append(band_exchange(outbound))
            else:
                held[chunk].append(outbound)

    def sum_blocks(returned):
        gathered = jnp.concatenate(returned, axis=1)
        return jnp.einsum("srk,srgpn->gkpn", one_hot, gathered, precision=lax.Precision.HIGHEST)

    home = []
    for chunk in range(len(bounds)):
        riders = held[chunk + 1] if chunk + 1 < len(bounds) else []
        summed, carried = line_reduce(sum_blocks(returned[chunk]), "grp", group_count, riders)
        if riders:
            returned[chunk + 1] = carried
        rows = summed.reshape(block_count * piece_rows, summed.shape[-1])
        home.append(lax.all_to_all(rows, "band", split_axis=1, concat_axis=0, tiled=True))
    return jnp.concatenate(home, axis=1)


def solution(mesh):
    placed = (P("grp", "band"), P(), P(("grp", "band"), None, None))
    return jax.shard_map(
        body, mesh=mesh, in_specs=placed, out_specs=P("grp", "band"), check_vma=False
    )
```

```python
import jax
import jax.numpy as jnp
from jax import lax
from jax.sharding import PartitionSpec as P

PRECISION = lax.Precision.HIGH


def band_exchange(outgoing):
    return lax.all_to_all(outgoing, "band", split_axis=0, concat_axis=0, tiled=True)


def line_gather(x, axis, count, riders=()):
    index = lax.axis_index(axis)
    spare = jnp.zeros((count + 1,) + x.shape, x.dtype)
    spare = lax.dynamic_update_index_in_dim(spare, x, index, 0)
    rightward, leftward = x, x
    carried = []
    for step in range(1, count):
        rider = step - 1 < len(riders)
        if rider:
            rightward, leftward, load = lax.optimization_barrier((rightward, leftward, riders[step - 1]))
        rightward = lax.ppermute(rightward, axis, [(i, i + 1) for i in range(step - 1, count - 1)])
        leftward = lax.ppermute(leftward, axis, [(i + 1, i) for i in range(0, count - step)])
        if rider:
            rightward, leftward, load = lax.optimization_barrier((rightward, leftward, band_exchange(load)))
            carried.append(load)
        from_left = jnp.where(index >= step, index - step, count)
        from_right = jnp.where(index + step < count, index + step, count)
        spare = lax.dynamic_update_index_in_dim(spare, rightward, from_left, 0)
        spare = lax.dynamic_update_index_in_dim(spare, leftward, from_right, 0)
    carried += [band_exchange(load) for load in riders[len(carried):]]
    return spare[:count], carried


def line_reduce(parts, axis, count, riders=()):
    index = lax.axis_index(axis)

    def part_for(target):
        return lax.dynamic_index_in_dim(parts, jnp.clip(target, 0, count - 1), 0, keepdims=False)

    rightward = jnp.zeros(parts.shape[1:], parts.dtype)
    leftward = jnp.zeros(parts.shape[1:], parts.dtype)
    carried = []
    for step in range(1, count):
        send_right = rightward + part_for(index + count - step)
        send_left = leftward + part_for(index - count + step)
        rider = step - 1 < len(riders)
        if rider:
            send_right, send_left, load = lax.optimization_barrier((send_right, send_left, riders[step - 1]))
        rightward = lax.ppermute(send_right, axis, [(i, i + 1) for i in range(0, step)])
        leftward = lax.ppermute(send_left, axis, [(i, i - 1) for i in range(count - step, count)])
        if rider:
            rightward, leftward, load = lax.optimization_barrier((rightward, leftward, band_exchange(load)))
            carried.append(load)
    carried += [band_exchange(load) for load in riders[len(carried):]]
    return part_for(index) + rightward + leftward, carried


def body(orbitals, requests, coulomb):
    group_count = lax.axis_size("grp")
    band_count = lax.axis_size("band")
    devices = group_count * band_count
    blk = coulomb.shape[1]
    piece_rows = blk // devices
    slot_count = coulomb.shape[0]
    block_count = orbitals.shape[0] // (band_count * piece_rows)
    quarter = orbitals.shape[1] // 4
    bounds = [(0, quarter), (quarter, 4 * quarter)]
    own_rows = [
        lax.all_to_all(orbitals[:, lo:hi], "band", split_axis=0, concat_axis=1, tiled=True)
        for lo, hi in bounds
    ]
    group_index = lax.axis_index("grp")
    band_index = lax.axis_index("band")
    group_requests = lax.dynamic_slice_in_dim(requests, group_index * band_count, band_count, 0)
    live = (group_requests >= 0).astype(jnp.float32)
    own_pairs = lax.dynamic_index_in_dim(group_requests, band_index, 0, keepdims=False)
    one_hot = (
        group_requests[:, :, None] == jnp.arange(block_count, dtype=jnp.int32)[None, None, :]
    ).astype(jnp.float32)

    def requested(pieces, slot):
        wanted = group_requests[:, 2 * slot : 2 * slot + 2]
        mask = live[None, :, 2 * slot : 2 * slot + 2, None, None]
        outgoing = jnp.take(pieces, jnp.maximum(wanted, 0), axis=1) * mask
        return outgoing.transpose(1, 2, 0, 3, 4)

    def shape_pieces(gathered):
        return gathered.reshape(group_count, block_count, piece_rows, gathered.shape[-1])

    pieces = shape_pieces(line_gather(own_rows[0], "grp", group_count)[0])
    arrived = []
    for chunk in range(1, len(bounds)):
        loads = [requested(pieces, slot) for slot in range(slot_count)]
        gathered, carried = line_gather(own_rows[chunk], "grp", group_count, loads)
        arrived.append(carried)
        pieces = shape_pieces(gathered)
    arrived.append([band_exchange(requested(pieces, slot)) for slot in range(slot_count)])
    returned = [[] for _ in bounds]
    held = [[] for _ in bounds]
    for slot in range(slot_count):
        rows = [
            part[slot].transpose(1, 2, 0, 3, 4).reshape(2, blk, part[slot].shape[-1]) for part in arrived
        ]
        density = sum(
            jnp.dot(r[0], r[1].T, precision=PRECISION, preferred_element_type=jnp.float32) for r in rows
        )
        kernel = density * coulomb[slot]
        scale = jnp.where(own_pairs[2 * slot] == own_pairs[2 * slot + 1], 0.5, 1.0)
        for chunk, r in enumerate(rows):
            onto_first = jnp.dot(kernel, r[1], precision=PRECISION, preferred_element_type=jnp.float32)
            onto_second = jnp.dot(kernel.T, r[0], precision=PRECISION, preferred_element_type=jnp.float32)
            outbound = (jnp.stack([onto_first, onto_second], 0) * scale).reshape(
                2, group_count, band_count, piece_rows, r.shape[-1]
            )
            outbound = outbound.transpose(2, 0, 1, 3, 4)
            if chunk == 0:
                returned[0].append(band_exchange(outbound))
            else:
                held[chunk].append(outbound)

    def sum_blocks(returned):
        gathered = jnp.concatenate(returned, axis=1)
        return jnp.einsum("srk,srgpn->gkpn", one_hot, gathered, precision=lax.Precision.HIGHEST)

    home = []
    for chunk in range(len(bounds)):
        riders = held[chunk + 1] if chunk + 1 < len(bounds) else []
        summed, carried = line_reduce(sum_blocks(returned[chunk]), "grp", group_count, riders)
        if riders:
            returned[chunk + 1] = carried
        rows = summed.reshape(block_count * piece_rows, summed.shape[-1])
        home.append(lax.all_to_all(rows, "band", split_axis=1, concat_axis=0, tiled=True))
    return jnp.concatenate(home, axis=1)


def solution(mesh):
    placed = (P("grp", "band"), P(), P(("grp", "band"), None, None))
    return jax.shard_map(
        body, mesh=mesh, in_specs=placed, out_specs=P("grp", "band"), check_vma=False
    )
```

```python
import jax
import jax.numpy as jnp
from jax import lax
from jax.sharding import PartitionSpec as P

PRECISION = lax.Precision.HIGH


def band_exchange(outgoing):
    return lax.all_to_all(outgoing, "band", split_axis=0, concat_axis=0, tiled=True)


def line_gather(x, axis, count, riders=()):
    index = lax.axis_index(axis)
    spare = jnp.zeros((count + 1,) + x.shape, x.dtype)
    spare = lax.dynamic_update_index_in_dim(spare, x, index, 0)
    rightward, leftward = x, x
    carried = []
    for step in range(1, count):
        rider = step - 1 < len(riders)
        if rider:
            rightward, leftward, load = lax.optimization_barrier((rightward, leftward, riders[step - 1]))
        rightward = lax.ppermute(rightward, axis, [(i, i + 1) for i in range(step - 1, count - 1)])
        leftward = lax.ppermute(leftward, axis, [(i + 1, i) for i in range(0, count - step)])
        if rider:
            rightward, leftward, load = lax.optimization_barrier((rightward, leftward, band_exchange(load)))
            carried.append(load)
        from_left = jnp.where(index >= step, index - step, count)
        from_right = jnp.where(index + step < count, index + step, count)
        spare = lax.dynamic_update_index_in_dim(spare, rightward, from_left, 0)
        spare = lax.dynamic_update_index_in_dim(spare, leftward, from_right, 0)
    carried += [band_exchange(load) for load in riders[len(carried):]]
    return spare[:count], carried


def line_reduce(parts, axis, count, riders=()):
    index = lax.axis_index(axis)

    def part_for(target):
        return lax.dynamic_index_in_dim(parts, jnp.clip(target, 0, count - 1), 0, keepdims=False)

    rightward = jnp.zeros(parts.shape[1:], parts.dtype)
    leftward = jnp.zeros(parts.shape[1:], parts.dtype)
    carried = []
    for step in range(1, count):
        send_right = rightward + part_for(index + count - step)
        send_left = leftward + part_for(index - count + step)
        rider = step - 1 < len(riders)
        if rider:
            send_right, send_left, load = lax.optimization_barrier((send_right, send_left, riders[step - 1]))
        rightward = lax.ppermute(send_right, axis, [(i, i + 1) for i in range(0, step)])
        leftward = lax.ppermute(send_left, axis, [(i, i - 1) for i in range(count - step, count)])
        if rider:
            rightward, leftward, load = lax.optimization_barrier((rightward, leftward, band_exchange(load)))
            carried.append(load)
    carried += [band_exchange(load) for load in riders[len(carried):]]
    return part_for(index) + rightward + leftward, carried


def body(orbitals, requests, coulomb):
    group_count = lax.axis_size("grp")
    band_count = lax.axis_size("band")
    devices = group_count * band_count
    blk = coulomb.shape[1]
    orbital_width = orbitals.shape[1] * band_count
    half = orbital_width // 2
    piece_rows = blk // devices
    slot_count = coulomb.shape[0]
    block_count = orbitals.shape[0] // (band_count * piece_rows)
    col_half = orbitals.shape[1] // 2
    own_rows = [
        lax.all_to_all(
            orbitals[:, h * col_half : (h + 1) * col_half], "band", split_axis=0, concat_axis=1, tiled=True
        )
        for h in range(2)
    ]
    group_index = lax.axis_index("grp")
    band_index = lax.axis_index("band")
    group_requests = lax.dynamic_slice_in_dim(requests, group_index * band_count, band_count, 0)
    live = (group_requests >= 0).astype(jnp.float32)
    own_pairs = lax.dynamic_index_in_dim(group_requests, band_index, 0, keepdims=False)
    one_hot = (
        group_requests[:, :, None] == jnp.arange(block_count, dtype=jnp.int32)[None, None, :]
    ).astype(jnp.float32)

    def requested(pieces, slot):
        wanted = group_requests[:, 2 * slot : 2 * slot + 2]
        mask = live[None, :, 2 * slot : 2 * slot + 2, None, None]
        outgoing = jnp.take(pieces, jnp.maximum(wanted, 0), axis=1) * mask
        return outgoing.transpose(1, 2, 0, 3, 4)

    def shape_pieces(gathered):
        return gathered.reshape(group_count, block_count, piece_rows, half)

    first_pieces = shape_pieces(line_gather(own_rows[0], "grp", group_count)[0])
    first_loads = [requested(first_pieces, slot) for slot in range(slot_count)]
    second_pieces, first_arrived = line_gather(own_rows[1], "grp", group_count, first_loads)
    second_pieces = shape_pieces(second_pieces)
    second_arrived = [band_exchange(requested(second_pieces, slot)) for slot in range(slot_count)]
    returned = [[], []]
    held = []
    for slot in range(slot_count):
        rows = [
            arrived.transpose(1, 2, 0, 3, 4).reshape(2, blk, half)
            for arrived in (first_arrived[slot], second_arrived[slot])
        ]
        density = sum(
            jnp.dot(r[0], r[1].T, precision=PRECISION, preferred_element_type=jnp.float32) for r in rows
        )
        kernel = density * coulomb[slot]
        scale = jnp.where(own_pairs[2 * slot] == own_pairs[2 * slot + 1], 0.5, 1.0)
        for h in range(2):
            onto_first = jnp.dot(kernel, rows[h][1], precision=PRECISION, preferred_element_type=jnp.float32)
            onto_second = jnp.dot(kernel.T, rows[h][0], precision=PRECISION, preferred_element_type=jnp.float32)
            outbound = (jnp.stack([onto_first, onto_second], 0) * scale).reshape(
                2, group_count, band_count, piece_rows, half
            )
            outbound = outbound.transpose(2, 0, 1, 3, 4)
            if h == 0:
                returned[0].append(band_exchange(outbound))
            else:
                held.append(outbound)

    def sum_blocks(returned):
        gathered = jnp.concatenate(returned, axis=1)
        return jnp.einsum("srk,srgpn->gkpn", one_hot, gathered, precision=PRECISION)

    first_home, second_returned = line_reduce(sum_blocks(returned[0]), "grp", group_count, held)
    second_home, _ = line_reduce(sum_blocks(second_returned), "grp", group_count)
    home = [
        lax.all_to_all(
            rows.reshape(block_count * piece_rows, half), "band", split_axis=1, concat_axis=0, tiled=True
        )
        for rows in (first_home, second_home)
    ]
    return jnp.concatenate(home, axis=1)


def solution(mesh):
    placed = (P("grp", "band"), P(), P(("grp", "band"), None, None))
    return jax.shard_map(
        body, mesh=mesh, in_specs=placed, out_specs=P("grp", "band"), check_vma=False
    )
```

```python
import jax
import jax.numpy as jnp
from jax import lax
from jax.sharding import PartitionSpec as P

PRECISION = lax.Precision.HIGH


def band_exchange(outgoing):
    return lax.all_to_all(outgoing, "band", split_axis=0, concat_axis=0, tiled=True)


def line_gather(x, axis, count, riders=()):
    index = lax.axis_index(axis)
    spare = jnp.zeros((count + 1,) + x.shape, x.dtype)
    spare = lax.dynamic_update_index_in_dim(spare, x, index, 0)
    rightward, leftward = x, x
    carried = []
    for step in range(1, count):
        rider = step - 1 < len(riders)
        if rider:
            rightward, leftward, load = lax.optimization_barrier((rightward, leftward, riders[step - 1]))
        rightward = lax.ppermute(rightward, axis, [(i, i + 1) for i in range(step - 1, count - 1)])
        leftward = lax.ppermute(leftward, axis, [(i + 1, i) for i in range(0, count - step)])
        if rider:
            rightward, leftward, load = lax.optimization_barrier((rightward, leftward, band_exchange(load)))
            carried.append(load)
        from_left = jnp.where(index >= step, index - step, count)
        from_right = jnp.where(index + step < count, index + step, count)
        spare = lax.dynamic_update_index_in_dim(spare, rightward, from_left, 0)
        spare = lax.dynamic_update_index_in_dim(spare, leftward, from_right, 0)
    carried += [band_exchange(load) for load in riders[len(carried):]]
    return spare[:count], carried


def line_reduce(parts, axis, count, riders=()):
    index = lax.axis_index(axis)

    def part_for(target):
        return lax.dynamic_index_in_dim(parts, jnp.clip(target, 0, count - 1), 0, keepdims=False)

    rightward = jnp.zeros(parts.shape[1:], parts.dtype)
    leftward = jnp.zeros(parts.shape[1:], parts.dtype)
    carried = []
    for step in range(1, count):
        send_right = rightward + part_for(index + count - step)
        send_left = leftward + part_for(index - count + step)
        rider = step - 1 < len(riders)
        if rider:
            send_right, send_left, load = lax.optimization_barrier((send_right, send_left, riders[step - 1]))
        rightward = lax.ppermute(send_right, axis, [(i, i + 1) for i in range(0, step)])
        leftward = lax.ppermute(send_left, axis, [(i, i - 1) for i in range(count - step, count)])
        if rider:
            rightward, leftward, load = lax.optimization_barrier((rightward, leftward, band_exchange(load)))
            carried.append(load)
    carried += [band_exchange(load) for load in riders[len(carried):]]
    return part_for(index) + rightward + leftward, carried


def body(orbitals, requests, coulomb):
    group_count = lax.axis_size("grp")
    band_count = lax.axis_size("band")
    devices = group_count * band_count
    blk = coulomb.shape[1]
    orbital_width = orbitals.shape[1] * band_count
    half = orbital_width // 2
    piece_rows = blk // devices
    slot_count = coulomb.shape[0]
    block_count = orbitals.shape[0] // (band_count * piece_rows)
    col_half = orbitals.shape[1] // 2
    own_rows = [
        lax.all_to_all(
            orbitals[:, h * col_half : (h + 1) * col_half], "band", split_axis=0, concat_axis=1, tiled=True
        )
        for h in range(2)
    ]
    group_index = lax.axis_index("grp")
    band_index = lax.axis_index("band")
    group_requests = lax.dynamic_slice_in_dim(requests, group_index * band_count, band_count, 0)
    live = (group_requests >= 0).astype(jnp.float32)
    own_pairs = lax.dynamic_index_in_dim(group_requests, band_index, 0, keepdims=False)
    one_hot = (
        group_requests[:, :, None] == jnp.arange(block_count, dtype=jnp.int32)[None, None, :]
    ).astype(jnp.float32)

    def requested(pieces, slot):
        wanted = group_requests[:, 2 * slot : 2 * slot + 2]
        mask = live[None, :, 2 * slot : 2 * slot + 2, None, None]
        outgoing = jnp.take(pieces, jnp.maximum(wanted, 0), axis=1) * mask
        return outgoing.transpose(1, 2, 0, 3, 4)

    def shape_pieces(gathered):
        return gathered.reshape(group_count, block_count, piece_rows, half)

    first_pieces = shape_pieces(line_gather(own_rows[0], "grp", group_count)[0])
    first_loads = [requested(first_pieces, slot) for slot in range(slot_count)]
    second_pieces, first_arrived = line_gather(own_rows[1], "grp", group_count, first_loads)
    second_pieces = shape_pieces(second_pieces)
    second_arrived = [band_exchange(requested(second_pieces, slot)) for slot in range(slot_count)]
    returned = [[], []]
    held = []
    for slot in range(slot_count):
        rows = [
            arrived.transpose(1, 2, 0, 3, 4).reshape(2, blk, half)
            for arrived in (first_arrived[slot], second_arrived[slot])
        ]
        density = sum(
            jnp.dot(r[0], r[1].T, precision=PRECISION, preferred_element_type=jnp.float32) for r in rows
        )
        scale = jnp.where(own_pairs[2 * slot] == own_pairs[2 * slot + 1], 0.5, 1.0)
        kernel = density * (coulomb[slot] * scale)
        for h in range(2):
            onto_first = jnp.dot(kernel, rows[h][1], precision=PRECISION, preferred_element_type=jnp.float32)
            onto_second = jnp.dot(kernel.T, rows[h][0], precision=PRECISION, preferred_element_type=jnp.float32)
            outbound = jnp.stack([onto_first, onto_second], 0).reshape(
                2, group_count, band_count, piece_rows, half
            )
            outbound = outbound.transpose(2, 0, 1, 3, 4)
            if h == 0:
                returned[0].append(band_exchange(outbound))
            else:
                held.append(outbound)

    def sum_blocks(returned):
        gathered = jnp.concatenate(returned, axis=1)
        return jnp.einsum("srk,srgpn->gkpn", one_hot, gathered, precision=PRECISION)

    first_home, second_returned = line_reduce(sum_blocks(returned[0]), "grp", group_count, held)
    second_home, _ = line_reduce(sum_blocks(second_returned), "grp", group_count)
    home = [
        lax.all_to_all(
            rows.reshape(block_count * piece_rows, half), "band", split_axis=1, concat_axis=0, tiled=True
        )
        for rows in (first_home, second_home)
    ]
    return jnp.concatenate(home, axis=1)


def solution(mesh):
    placed = (P("grp", "band"), P(), P(("grp", "band"), None, None))
    return jax.shard_map(
        body, mesh=mesh, in_specs=placed, out_specs=P("grp", "band"), check_vma=False
    )
```

```python
import jax
import jax.numpy as jnp
from jax import lax
from jax.sharding import PartitionSpec as P

PRECISION = lax.Precision.HIGH


def band_exchange(outgoing):
    return lax.all_to_all(outgoing, "band", split_axis=0, concat_axis=0, tiled=True)


def line_gather(x, axis, count, riders=()):
    index = lax.axis_index(axis)
    spare = jnp.zeros((count + 1,) + x.shape, x.dtype)
    spare = lax.dynamic_update_index_in_dim(spare, x, index, 0)
    rightward, leftward = x, x
    carried = []
    for step in range(1, count):
        rider = step - 1 < len(riders)
        if rider:
            rightward, leftward, load = lax.optimization_barrier((rightward, leftward, riders[step - 1]))
        rightward = lax.ppermute(rightward, axis, [(i, i + 1) for i in range(step - 1, count - 1)])
        leftward = lax.ppermute(leftward, axis, [(i + 1, i) for i in range(0, count - step)])
        if rider:
            rightward, leftward, load = lax.optimization_barrier((rightward, leftward, band_exchange(load)))
            carried.append(load)
        from_left = jnp.where(index >= step, index - step, count)
        from_right = jnp.where(index + step < count, index + step, count)
        spare = lax.dynamic_update_index_in_dim(spare, rightward, from_left, 0)
        spare = lax.dynamic_update_index_in_dim(spare, leftward, from_right, 0)
    carried += [band_exchange(load) for load in riders[len(carried):]]
    return spare[:count], carried


def line_reduce(parts, axis, count, riders=()):
    index = lax.axis_index(axis)

    def part_for(target):
        return lax.dynamic_index_in_dim(parts, jnp.clip(target, 0, count - 1), 0, keepdims=False)

    rightward = jnp.zeros(parts.shape[1:], parts.dtype)
    leftward = jnp.zeros(parts.shape[1:], parts.dtype)
    carried = []
    for step in range(1, count):
        send_right = rightward + part_for(index + count - step)
        send_left = leftward + part_for(index - count + step)
        rider = step - 1 < len(riders)
        if rider:
            send_right, send_left, load = lax.optimization_barrier((send_right, send_left, riders[step - 1]))
        rightward = lax.ppermute(send_right, axis, [(i, i + 1) for i in range(0, step)])
        leftward = lax.ppermute(send_left, axis, [(i, i - 1) for i in range(count - step, count)])
        if rider:
            rightward, leftward, load = lax.optimization_barrier((rightward, leftward, band_exchange(load)))
            carried.append(load)
    carried += [band_exchange(load) for load in riders[len(carried):]]
    return part_for(index) + rightward + leftward, carried


def body(orbitals, requests, coulomb):
    group_count = lax.axis_size("grp")
    band_count = lax.axis_size("band")
    devices = group_count * band_count
    blk = coulomb.shape[1]
    orbital_width = orbitals.shape[1] * band_count
    half = orbital_width // 2
    piece_rows = blk // devices
    slot_count = coulomb.shape[0]
    block_count = orbitals.shape[0] // (band_count * piece_rows)
    col_half = orbitals.shape[1] // 2
    own_rows = [
        lax.all_to_all(
            orbitals[:, h * col_half : (h + 1) * col_half], "band", split_axis=0, concat_axis=1, tiled=True
        )
        for h in range(2)
    ]
    group_index = lax.axis_index("grp")
    band_index = lax.axis_index("band")
    group_requests = lax.dynamic_slice_in_dim(requests, group_index * band_count, band_count, 0)
    own_pairs = lax.dynamic_index_in_dim(group_requests, band_index, 0, keepdims=False)
    one_hot = (
        group_requests[:, :, None] == jnp.arange(block_count, dtype=jnp.int32)[None, None, :]
    ).astype(jnp.float32)

    def requested(pieces, slot):
        wanted = group_requests[:, 2 * slot : 2 * slot + 2]
        wanted = jnp.where(wanted >= 0, wanted, block_count)
        outgoing = jnp.take(pieces, wanted, axis=1, mode="fill", fill_value=0.0)
        return outgoing.transpose(1, 2, 0, 3, 4)

    def shape_pieces(gathered):
        return gathered.reshape(group_count, block_count, piece_rows, half)

    first_pieces = shape_pieces(line_gather(own_rows[0], "grp", group_count)[0])
    first_loads = [requested(first_pieces, slot) for slot in range(slot_count)]
    second_pieces, first_arrived = line_gather(own_rows[1], "grp", group_count, first_loads)
    second_pieces = shape_pieces(second_pieces)
    second_arrived = [band_exchange(requested(second_pieces, slot)) for slot in range(slot_count)]
    returned = [[], []]
    held = []
    for slot in range(slot_count):
        rows = [
            arrived.transpose(1, 2, 0, 3, 4).reshape(2, blk, half)
            for arrived in (first_arrived[slot], second_arrived[slot])
        ]
        density = sum(
            jnp.dot(r[0], r[1].T, precision=PRECISION, preferred_element_type=jnp.float32) for r in rows
        )
        scale = jnp.where(own_pairs[2 * slot] == own_pairs[2 * slot + 1], 0.5, 1.0)
        kernel = density * (coulomb[slot] * scale)
        for h in range(2):
            onto_first = jnp.dot(kernel, rows[h][1], precision=PRECISION, preferred_element_type=jnp.float32)
            onto_second = jnp.dot(kernel.T, rows[h][0], precision=PRECISION, preferred_element_type=jnp.float32)
            outbound = jnp.stack([onto_first, onto_second], 0).reshape(
                2, group_count, band_count, piece_rows, half
            )
            outbound = outbound.transpose(2, 0, 1, 3, 4)
            if h == 0:
                returned[0].append(band_exchange(outbound))
            else:
                held.append(outbound)

    def sum_blocks(returned):
        gathered = jnp.concatenate(returned, axis=1)
        return jnp.einsum("srk,srgpn->gkpn", one_hot, gathered, precision=PRECISION)

    first_home, second_returned = line_reduce(sum_blocks(returned[0]), "grp", group_count, held)
    second_home, _ = line_reduce(sum_blocks(second_returned), "grp", group_count)
    home = [
        lax.all_to_all(
            rows.reshape(block_count * piece_rows, half), "band", split_axis=1, concat_axis=0, tiled=True
        )
        for rows in (first_home, second_home)
    ]
    return jnp.concatenate(home, axis=1)


def solution(mesh):
    placed = (P("grp", "band"), P(), P(("grp", "band"), None, None))
    return jax.shard_map(
        body, mesh=mesh, in_specs=placed, out_specs=P("grp", "band"), check_vma=False
    )
```

```python
import jax
import jax.numpy as jnp
from jax import lax
from jax.sharding import PartitionSpec as P

PRECISION = lax.Precision.HIGH


def band_exchange(outgoing):
    return lax.all_to_all(outgoing, "band", split_axis=0, concat_axis=0, tiled=True)


def line_gather(x, axis, count, riders=()):
    index = lax.axis_index(axis)
    spare = jnp.zeros((count + 1,) + x.shape, x.dtype)
    spare = lax.dynamic_update_index_in_dim(spare, x, index, 0)
    rightward, leftward = x, x
    carried = []
    for step in range(1, count):
        rider = step - 1 < len(riders)
        if rider:
            rightward, leftward, load = lax.optimization_barrier((rightward, leftward, riders[step - 1]))
        rightward = lax.ppermute(rightward, axis, [(i, i + 1) for i in range(step - 1, count - 1)])
        leftward = lax.ppermute(leftward, axis, [(i + 1, i) for i in range(0, count - step)])
        if rider:
            rightward, leftward, load = lax.optimization_barrier((rightward, leftward, band_exchange(load)))
            carried.append(load)
        from_left = jnp.where(index >= step, index - step, count)
        from_right = jnp.where(index + step < count, index + step, count)
        spare = lax.dynamic_update_index_in_dim(spare, rightward, from_left, 0)
        spare = lax.dynamic_update_index_in_dim(spare, leftward, from_right, 0)
    carried += [band_exchange(load) for load in riders[len(carried):]]
    return spare[:count], carried


def line_reduce(parts, axis, count, riders=()):
    index = lax.axis_index(axis)

    def part_for(target):
        return lax.dynamic_index_in_dim(parts, jnp.clip(target, 0, count - 1), 0, keepdims=False)

    rightward = jnp.zeros(parts.shape[1:], parts.dtype)
    leftward = jnp.zeros(parts.shape[1:], parts.dtype)
    carried = []
    for step in range(1, count):
        send_right = rightward + part_for(index + count - step)
        send_left = leftward + part_for(index - count + step)
        rider = step - 1 < len(riders)
        if rider:
            send_right, send_left, load = lax.optimization_barrier((send_right, send_left, riders[step - 1]))
        rightward = lax.ppermute(send_right, axis, [(i, i + 1) for i in range(0, step)])
        leftward = lax.ppermute(send_left, axis, [(i, i - 1) for i in range(count - step, count)])
        if rider:
            rightward, leftward, load = lax.optimization_barrier((rightward, leftward, band_exchange(load)))
            carried.append(load)
    carried += [band_exchange(load) for load in riders[len(carried):]]
    return part_for(index) + rightward + leftward, carried


def body(orbitals, requests, coulomb):
    group_count = lax.axis_size("grp")
    band_count = lax.axis_size("band")
    devices = group_count * band_count
    blk = coulomb.shape[1]
    orbital_width = orbitals.shape[1] * band_count
    half = orbital_width // 2
    piece_rows = blk // devices
    slot_count = coulomb.shape[0]
    block_count = orbitals.shape[0] // (band_count * piece_rows)
    col_half = orbitals.shape[1] // 2
    own_rows = [
        lax.all_to_all(
            orbitals[:, h * col_half : (h + 1) * col_half], "band", split_axis=0, concat_axis=1, tiled=True
        )
        for h in range(2)
    ]
    group_index = lax.axis_index("grp")
    band_index = lax.axis_index("band")
    group_requests = lax.dynamic_slice_in_dim(requests, group_index * band_count, band_count, 0)
    own_pairs = lax.dynamic_index_in_dim(group_requests, band_index, 0, keepdims=False)
    one_hot = (
        group_requests[:, :, None] == jnp.arange(block_count, dtype=jnp.int32)[None, None, :]
    ).astype(jnp.float32)

    def requested(pieces, slot):
        wanted = group_requests[:, 2 * slot : 2 * slot + 2]
        wanted = jnp.where(wanted >= 0, wanted, block_count)
        return jnp.take(pieces, wanted, axis=0, mode="fill", fill_value=0.0)

    def shape_pieces(gathered):
        return gathered.reshape(group_count, block_count, piece_rows, half).transpose(1, 0, 2, 3)

    first_pieces = shape_pieces(line_gather(own_rows[0], "grp", group_count)[0])
    first_loads = [requested(first_pieces, slot) for slot in range(slot_count)]
    second_pieces, first_arrived = line_gather(own_rows[1], "grp", group_count, first_loads)
    second_pieces = shape_pieces(second_pieces)
    second_arrived = [band_exchange(requested(second_pieces, slot)) for slot in range(slot_count)]
    returned = [[], []]
    held = []
    for slot in range(slot_count):
        rows = [
            arrived.transpose(1, 2, 0, 3, 4).reshape(2, blk, half)
            for arrived in (first_arrived[slot], second_arrived[slot])
        ]
        density = sum(
            jnp.dot(r[0], r[1].T, precision=PRECISION, preferred_element_type=jnp.float32) for r in rows
        )
        scale = jnp.where(own_pairs[2 * slot] == own_pairs[2 * slot + 1], 0.5, 1.0)
        kernel = density * (coulomb[slot] * scale)
        for h in range(2):
            onto_first = jnp.dot(kernel, rows[h][1], precision=PRECISION, preferred_element_type=jnp.float32)
            onto_second = jnp.dot(kernel.T, rows[h][0], precision=PRECISION, preferred_element_type=jnp.float32)
            outbound = jnp.stack([onto_first, onto_second], 0).reshape(
                2, group_count, band_count, piece_rows, half
            )
            outbound = outbound.transpose(2, 0, 1, 3, 4)
            if h == 0:
                returned[0].append(band_exchange(outbound))
            else:
                held.append(outbound)

    def sum_blocks(returned):
        gathered = jnp.concatenate(returned, axis=1)
        return jnp.einsum("srk,srgpn->gkpn", one_hot, gathered, precision=PRECISION)

    first_home, second_returned = line_reduce(sum_blocks(returned[0]), "grp", group_count, held)
    second_home, _ = line_reduce(sum_blocks(second_returned), "grp", group_count)
    home = [
        lax.all_to_all(
            rows.reshape(block_count * piece_rows, half), "band", split_axis=1, concat_axis=0, tiled=True
        )
        for rows in (first_home, second_home)
    ]
    return jnp.concatenate(home, axis=1)


def solution(mesh):
    placed = (P("grp", "band"), P(), P(("grp", "band"), None, None))
    return jax.shard_map(
        body, mesh=mesh, in_specs=placed, out_specs=P("grp", "band"), check_vma=False
    )
```
